512 devices in a mesh: date: 8 (over z), trade: 64 (over x, y, core).
Axes of the slice: x: 4, y: 8, z: 8, core: 2. Of those that a mesh axis runs over, the one named last changes fastest.
Arguments:
- initial_term_structure: float32 [48], replicated, may hold values from 0.01 to 0.06
- long_level: float32 [48], replicated, may hold values from 0.01 to 0.07
- reversion: float32 [48], replicated, may hold values from 0.02 to 2
- volatility: float32 [48], replicated, may hold values from 0.002 to 0.01
- mixing: float32 [48, 48], replicated, may hold values from -0.875 to 0.875
- shocks: float32 [16, 48, 512], P('date'), may hold values from -6 to 6
- cashflows: bfloat16 [48, 524288], P(None, 'trade'), may hold values from -0.01953125 to 0.01953125
- maturity: int32 [524288], P('trade'), may hold values from 1 to 16, as said below
- netting: int32 [524288], P('trade'), may hold values from 0 to 255
Outputs:
- exposure: float32 [16, 256], P('date', 'trade')
The draws below stay inside these ranges and needn't reach their ends.
Inputs may be any that keep to these rules, and one draw needn't show every extreme that they name: Trades are grouped by maturity along trade: the trades held by one device mature within a narrow band of dates that rises with the device's index.
All inputs are finite; a program needn't handle non-finite values.
Results may differ from the reference program's by a relative error of at most 0.003.
Values may be sent and summed in bfloat16 or wider, within the bound.
No kernel may reach another device: no remote copies, remote signals or barrier semaphores. Data moves between devices by JAX's collectives and lax.ppermute only.
A program may use at most 64 MiB of HBM per device.

```python
import math
import jax
import jax.numpy as jnp
from jax import lax

FACTORS = 48
PATHS = 512
TR_DEV = 8192
SETS_DEV = 4
DATES = 16
CONTRACT_COUNT = 524288
SETS = 256


def draw_maturity(key, part):
    index = jnp.arange(CONTRACT_COUNT, dtype=jnp.int32)
    owner = index // TR_DEV
    holders = CONTRACT_COUNT // TR_DEV
    lower = 1 + owner * (DATES - 1) // holders
    upper = 1 + (owner + 1) * (DATES - 1) // holders
    raw = jax.random.randint(key, (CONTRACT_COUNT,), 0, 1 << 20, dtype=jnp.int32)
    picked = lower + raw % (upper - lower + 1)
    return jnp.where(index % TR_DEV == 0, upper, picked).astype(jnp.int32)


def touch_ends(result, stream_key, smallest, high):
    dims = result.shape
    place = [jax.random.randint(jax.random.fold_in(stream_key, axis), (), 0, dims[axis]) for axis in range(len(dims))]
    result = result.at[tuple(place)].set(smallest)
    longest = dims.index(max(dims))
    place[longest] = (place[longest] + 1) % dims[longest]
    return result.at[tuple(place)].set(high)


def shard_levels(rng, shape, split, smallest, high):
    factor_of = 1.0
    for position, blocks in split:
        draws = jax.random.uniform(jax.random.fold_in(jax.random.fold_in(rng, 6), position), (blocks,), jnp.float32, smallest / len(split), high / len(split))
        factor_of = factor_of * jnp.repeat(jnp.exp(draws), shape[position] // blocks).reshape((-1,) + (1,) * (len(shape) - 1 - position))
    return factor_of


def centred(stream_key, dims, scale, bound, pieces=(), kind=jnp.bfloat16):
    array = jax.random.normal(stream_key, dims, jnp.float32) * scale
    if len(pieces) > 0:
        array = shard_levels(stream_key, dims, pieces, -0.22, 0.18) * array
    return jnp.clip(array, min=-bound, max=bound).astype(kind)


def setup_inputs(seed: int = 0) -> dict:
    keys = jax.random.split(jax.random.key(seed), 10)
    initial_term_structure = jnp.clip(jax.random.uniform(keys[0], (FACTORS,), jnp.float32, 0.01, 0.06), 0.01, 0.06)
    long_level = jnp.clip(jax.random.uniform(keys[1], (FACTORS,), jnp.float32, 0.01, 0.07), 0.01, 0.07)
    reversion = jnp.clip(jnp.exp(jax.random.uniform(keys[2], (FACTORS,), jnp.float32, math.log(0.02), math.log(2.0))), 0.02, 2.0)
    volatility = jnp.clip(jnp.exp(jax.random.uniform(keys[3], (FACTORS,), jnp.float32, math.log(0.002), math.log(0.01))), 0.002, 0.01)
    mixing = centred(keys[4], (FACTORS, FACTORS), FACTORS ** -0.5, 0.875, (), jnp.float32)
    shocks = centred(keys[5], (DATES, FACTORS, PATHS), 1.0, 6.0, ((0, 8),), jnp.float32)
    cashflows = centred(keys[6], (FACTORS, CONTRACT_COUNT), (FACTORS * TR_DEV // SETS_DEV) ** -0.5, 0.01953125, ((1, 64),))
    maturity = draw_maturity(jax.random.fold_in(keys[9], 71), 0)
    netting = touch_ends(jax.random.randint(keys[8], (CONTRACT_COUNT,), 0, SETS), jax.random.fold_in(keys[8], 1), 0, SETS - 1).astype(jnp.int32)
    return {"initial_term_structure": initial_term_structure, "long_level": long_level, "reversion": reversion, "volatility": volatility, "mixing": mixing, "shocks": shocks, "cashflows": cashflows, "maturity": maturity, "netting": netting}


def reference(initial_term_structure, long_level, reversion, volatility, mixing, shocks, cashflows, maturity, netting):
    decay = jnp.exp(-0.25 * reversion)
    drift = (1.0 - decay) * long_level
    tenor = 0.25 * (jnp.arange(FACTORS, dtype=jnp.int32).astype(jnp.float32) + 1.0)
    y_start = jnp.broadcast_to(initial_term_structure[:, None], (FACTORS, PATHS)).astype(jnp.float32)

    def advance(y_prev, shock):
        moved = jnp.dot(mixing, shock, precision=lax.Precision.HIGHEST)
        y_next = decay[:, None] * y_prev + drift[:, None] + volatility[:, None] * moved
        return y_next, y_next

    _, yields = lax.scan(advance, y_start, shocks)
    dates = jnp.arange(DATES, dtype=jnp.int32)
    cash_rows = cashflows.astype(jnp.float32).T

    def per_date(item):
        y_now, valuation_date = item
        discount = jnp.exp(-y_now * tenor[:, None]).astype(jnp.bfloat16).astype(jnp.float32)
        weight = jnp.maximum(maturity - valuation_date, 0).astype(jnp.float32) / maturity.astype(jnp.float32)
        set_rows = jax.ops.segment_sum(cash_rows * weight[:, None], netting, SETS)
        value = jnp.dot(set_rows, discount, precision=lax.Precision.HIGHEST)
        return jnp.mean(jnp.maximum(value, 0.0), axis=1)

    return lax.map(per_date, (yields, dates))
```

```python
import jax
import jax.numpy as jnp
from jax import lax
from jax.sharding import PartitionSpec as P

SETS_DEV = 4
RS_MODE = "a2a"
Y_MODE = "permute"


def from_behind(array, axis, by):
    devices = lax.axis_size(axis)
    pairs = [(i, i + by) for i in range(devices) if 0 <= i + by < devices]
    return lax.ppermute(array, axis, pairs)


def per_device(
    initial_term_structure,
    long_level,
    reversion,
    volatility,
    mixing,
    shocks,
    cashflows,
    maturity,
    netting,
):
    section = shocks.shape[0]
    factors = shocks.shape[1]
    paths = shocks.shape[2]
    dates_n = lax.axis_size("date")
    trades_n = lax.axis_size("trade")
    sets_all = SETS_DEV * trades_n
    date_index = lax.axis_index("date")

    trades = cashflows.shape[1]
    mat_f = maturity.astype(jnp.float32)
    weights = []
    for step in range(section):
        valuation_date = date_index * section + step
        weights.append(
            jnp.maximum(maturity - valuation_date, 0).astype(jnp.float32) / mat_f
        )
    cash_f = cashflows.astype(jnp.float32)
    weighted = jnp.concatenate([cash_f * w[None, :] for w in weights], axis=0)
    member = (
        lax.broadcasted_iota(jnp.int32, (sets_all, trades), 0) == netting[None, :]
    ).astype(jnp.bfloat16)
    hi_f = lax.reduce_precision(weighted, exponent_bits=8, mantissa_bits=7)
    hi = hi_f.astype(jnp.bfloat16)
    lo = (weighted - hi_f).astype(jnp.bfloat16)
    dims = (((1,), (1,)), ((), ()))
    rows = lax.dot_general(member, hi, dims, preferred_element_type=jnp.float32)
    rows = rows + lax.dot_general(member, lo, dims, preferred_element_type=jnp.float32)
    if RS_MODE == "scatter":
        owned = lax.psum_scatter(rows, "trade", scatter_dimension=0, tiled=True)
    elif RS_MODE == "a2a":
        parts = rows.reshape(trades_n, SETS_DEV, section * factors)
        got = lax.all_to_all(parts, "trade", 0, 0, tiled=True)
        owned = jnp.sum(got, axis=0)
    else:
        whole = lax.psum(rows, "trade")
        owned = lax.dynamic_slice_in_dim(
            whole, lax.axis_index("trade") * SETS_DEV, SETS_DEV, 0
        )

    decay = jnp.exp(-0.25 * reversion)[:, None]
    drift = ((1.0 - jnp.exp(-0.25 * reversion)) * long_level)[:, None]
    tenor = 0.25 * (jnp.arange(factors, dtype=jnp.float32) + 1.0)
    y_start = jnp.broadcast_to(initial_term_structure[:, None], (factors, paths))
    offsets = []
    powers = []
    running = jnp.zeros((factors, paths), jnp.float32)
    steady = jnp.zeros((factors, 1), jnp.float32)
    power = jnp.ones((factors, 1), jnp.float32)
    for step in range(section):
        moved = jnp.dot(mixing, shocks[step], precision=lax.Precision.HIGHEST)
        running = decay * running + drift + volatility[:, None] * moved
        steady = decay * steady + drift
        power = power * decay
        offsets.append(running)
        powers.append(power)
    multiplier = powers[-1]
    noise = (offsets[-1] - steady).astype(jnp.bfloat16)
    if Y_MODE == "permute":
        arrived = [None] + [
            from_behind(noise, "date", by).astype(jnp.float32)
            for by in range(1, dates_n)
        ]
    else:
        gathered = lax.all_gather(noise, "date", axis=0, tiled=False)
        arrived = [None] + [
            lax.dynamic_index_in_dim(
                gathered, jnp.maximum(date_index - by, 0), 0, keepdims=False
            ).astype(jnp.float32)
            for by in range(1, dates_n)
        ]
    incoming_state = y_start
    for by in range(dates_n - 1, 0, -1):
        stepped = multiplier * incoming_state + (steady + arrived[by])
        incoming_state = jnp.where(by <= date_index, stepped, incoming_state)

    values = []
    for step in range(section):
        y_now = powers[step] * incoming_state + offsets[step]
        discount = jnp.exp(-y_now * tenor[:, None]).astype(jnp.bfloat16).astype(jnp.float32)
        set_rows = owned[:, step * factors:(step + 1) * factors]
        value = jnp.dot(set_rows, discount, precision=lax.Precision.HIGHEST)
        values.append(jnp.mean(jnp.maximum(value, 0.0), axis=1))
    return jnp.stack(values)


def solution(mesh):
    return jax.shard_map(
        per_device,
        mesh=mesh,
        in_specs=(
            P(),
            P(),
            P(),
            P(),
            P(),
            P("date", None, None),
            P(None, "trade"),
            P("trade"),
            P("trade"),
        ),
        out_specs=P("date", "trade"),
        check_vma=False,
    )
```

```python
import jax
import jax.numpy as jnp
from jax import lax
from jax.sharding import PartitionSpec as P

SETS_DEV = 4
RS_MODE = "a2a"
Y_MODE = "scan"
TRADE_SPLIT = ()
TRADE_AXES = ("trade",)


def from_behind(array, axis, by):
    devices = lax.axis_size(axis)
    pairs = [(i, i + by) for i in range(devices) if 0 <= i + by < devices]
    return lax.ppermute(array, axis, pairs)


def per_device(
    initial_term_structure,
    long_level,
    reversion,
    volatility,
    mixing,
    shocks,
    cashflows,
    maturity,
    netting,
):
    section = shocks.shape[0]
    factors = shocks.shape[1]
    paths = shocks.shape[2]
    dates_n = lax.axis_size("date")
    date_index = lax.axis_index("date")
    trades_n = 1
    for axis in TRADE_AXES:
        trades_n *= lax.axis_size(axis)
    sets_all = SETS_DEV * trades_n

    trades = cashflows.shape[1]
    mat_f = maturity.astype(jnp.float32)
    weights = []
    for step in range(section):
        valuation_date = date_index * section + step
        weights.append(
            jnp.maximum(maturity - valuation_date, 0).astype(jnp.float32) / mat_f
        )
    cash_f = cashflows.astype(jnp.float32)
    weighted = jnp.concatenate([cash_f * w[None, :] for w in weights], axis=0)
    member = (
        lax.broadcasted_iota(jnp.int32, (sets_all, trades), 0) == netting[None, :]
    ).astype(jnp.bfloat16)
    hi_f = lax.reduce_precision(weighted, exponent_bits=8, mantissa_bits=7)
    hi = hi_f.astype(jnp.bfloat16)
    lo = (weighted - hi_f).astype(jnp.bfloat16)
    dims = (((1,), (1,)), ((), ()))
    rows = lax.dot_general(member, hi, dims, preferred_element_type=jnp.float32)
    rows = rows + lax.dot_general(member, lo, dims, preferred_element_type=jnp.float32)
    if RS_MODE == "scatter":
        owned = lax.psum_scatter(rows, "trade", scatter_dimension=0, tiled=True)
    elif RS_MODE == "a2a":
        owned = rows
        for axis in TRADE_AXES:
            peers = lax.axis_size(axis)
            parts = owned.reshape(peers, owned.shape[0] // peers, owned.shape[1])
            owned = jnp.sum(lax.all_to_all(parts, axis, 0, 0, tiled=True), axis=0)
    else:
        whole = lax.psum(rows, "trade")
        owned = lax.dynamic_slice_in_dim(
            whole, lax.axis_index("trade") * SETS_DEV, SETS_DEV, 0
        )

    decay = jnp.exp(-0.25 * reversion)[:, None]
    drift = ((1.0 - jnp.exp(-0.25 * reversion)) * long_level)[:, None]
    tenor = 0.25 * (jnp.arange(factors, dtype=jnp.float32) + 1.0)
    y_start = jnp.broadcast_to(initial_term_structure[:, None], (factors, paths))
    offsets = []
    powers = []
    running = jnp.zeros((factors, paths), jnp.float32)
    steady = jnp.zeros((factors, 1), jnp.float32)
    power = jnp.ones((factors, 1), jnp.float32)
    for step in range(section):
        moved = jnp.dot(mixing, shocks[step], precision=lax.Precision.HIGHEST)
        running = decay * running + drift + volatility[:, None] * moved
        steady = decay * steady + drift
        power = power * decay
        offsets.append(running)
        powers.append(power)
    multiplier = powers[-1]
    noise = (offsets[-1] - steady).astype(jnp.bfloat16)
    if Y_MODE == "permute":
        arrived = [None] + [
            from_behind(noise, "date", by).astype(jnp.float32)
            for by in range(1, dates_n)
        ]
    elif Y_MODE == "a2a":
        sent = jnp.broadcast_to(noise[None], (dates_n,) + noise.shape)
        got = lax.all_to_all(sent, "date", 0, 0, tiled=True)
        arrived = [None] + [
            lax.dynamic_index_in_dim(
                got, jnp.maximum(date_index - by, 0), 0, keepdims=False
            ).astype(jnp.float32)
            for by in range(1, dates_n)
        ]
    elif Y_MODE == "scan":
        arrived = None
    else:
        gathered = lax.all_gather(noise, "date", axis=0, tiled=False)
        arrived = [None] + [
            lax.dynamic_index_in_dim(
                gathered, jnp.maximum(date_index - by, 0), 0, keepdims=False
            ).astype(jnp.float32)
            for by in range(1, dates_n)
        ]
    incoming_state = y_start
    if Y_MODE == "scan":
        inclusive = noise.astype(jnp.float32)
        exclusive = jnp.zeros_like(inclusive)
        by = 1
        while by < dates_n:
            far = from_behind(inclusive.astype(jnp.bfloat16), "date", by).astype(jnp.float32)
            exclusive = exclusive + multiplier ** (by - 1) * far
            inclusive = inclusive + multiplier ** by * far
            by *= 2
        for by in range(dates_n - 1, 0, -1):
            stepped = multiplier * incoming_state + steady
            incoming_state = jnp.where(by <= date_index, stepped, incoming_state)
        incoming_state = incoming_state + exclusive
    for by in range(dates_n - 1, 0, -1) if Y_MODE != "scan" else ():
        stepped = multiplier * incoming_state + (steady + arrived[by])
        incoming_state = jnp.where(by <= date_index, stepped, incoming_state)

    values = []
    for step in range(section):
        y_now = powers[step] * incoming_state + offsets[step]
        discount = jnp.exp(-y_now * tenor[:, None]).astype(jnp.bfloat16).astype(jnp.float32)
        set_rows = owned[:, step * factors:(step + 1) * factors]
        value = jnp.dot(set_rows, discount, precision=lax.Precision.HIGHEST)
        values.append(jnp.mean(jnp.maximum(value, 0.0), axis=1))
    return jnp.stack(values)


def solution(mesh):
    trade = "trade"
    if TRADE_SPLIT:
        devices = mesh.devices.reshape((mesh.devices.shape[0],) + TRADE_SPLIT)
        mesh = jax.sharding.Mesh(devices, ("date",) + TRADE_AXES)
        trade = TRADE_AXES
    return jax.shard_map(
        per_device,
        mesh=mesh,
        in_specs=(
            P(),
            P(),
            P(),
            P(),
            P(),
            P("date", None, None),
            P(None, trade),
            P(trade),
            P(trade),
        ),
        out_specs=P("date", trade),
        check_vma=False,
    )
```

```python
import jax
import jax.numpy as jnp
from jax import lax
from jax.sharding import PartitionSpec as P

SETS_DEV = 4
RS_MODE = "a2a"
Y_MODE = "scan"
ORDER_TIE = False
TRADE_SPLIT = ()
TRADE_AXES = ("trade",)


def from_behind(array, axis, by):
    devices = lax.axis_size(axis)
    pairs = [(i, i + by) for i in range(devices) if 0 <= i + by < devices]
    return lax.ppermute(array, axis, pairs)


def per_device(
    initial_term_structure,
    long_level,
    reversion,
    volatility,
    mixing,
    shocks,
    cashflows,
    maturity,
    netting,
):
    section = shocks.shape[0]
    factors = shocks.shape[1]
    paths = shocks.shape[2]
    dates_n = lax.axis_size("date")
    date_index = lax.axis_index("date")
    trades_n = 1
    for axis in TRADE_AXES:
        trades_n *= lax.axis_size(axis)
    sets_all = SETS_DEV * trades_n

    trades = cashflows.shape[1]
    mat_f = maturity.astype(jnp.float32)
    weights = []
    for step in range(section):
        valuation_date = date_index * section + step
        weights.append(
            jnp.maximum(maturity - valuation_date, 0).astype(jnp.float32) / mat_f
        )
    cash_f = cashflows.astype(jnp.float32)
    weighted = jnp.concatenate([cash_f * w[None, :] for w in weights], axis=0)
    member = (
        lax.broadcasted_iota(jnp.int32, (sets_all, trades), 0) == netting[None, :]
    ).astype(jnp.bfloat16)
    hi_f = lax.reduce_precision(weighted, exponent_bits=8, mantissa_bits=7)
    hi = hi_f.astype(jnp.bfloat16)
    lo = (weighted - hi_f).astype(jnp.bfloat16)
    dims = (((1,), (1,)), ((), ()))
    both = lax.dot_general(
        member, jnp.concatenate([hi, lo], axis=0), dims, preferred_element_type=jnp.float32
    )
    rows = both[:, : hi.shape[0]] + both[:, hi.shape[0]:]
    if RS_MODE == "scatter":
        owned = lax.psum_scatter(rows, "trade", scatter_dimension=0, tiled=True)
    elif RS_MODE == "pair":
        chips_axis, core_axis = TRADE_AXES
        chips = lax.axis_size(chips_axis)
        core = lax.axis_index(core_axis)
        by_core = rows.reshape(chips, 2, SETS_DEV, rows.shape[1])
        keep = lax.dynamic_index_in_dim(by_core, core, 1, keepdims=False)
        give = lax.dynamic_index_in_dim(by_core, 1 - core, 1, keepdims=False)
        mine = keep + lax.ppermute(give, core_axis, [(0, 1), (1, 0)])
        owned = jnp.sum(lax.all_to_all(mine, chips_axis, 0, 0, tiled=True), axis=0)
    elif RS_MODE == "a2a":
        owned = rows
        for axis in TRADE_AXES:
            peers = lax.axis_size(axis)
            parts = owned.reshape(peers, owned.shape[0] // peers, owned.shape[1])
            if ORDER_TIE == "rows_first":
                parts, shocks = lax.optimization_barrier((parts, shocks))
            if ORDER_TIE == "scan_first":
                owned = parts
                break
            owned = jnp.sum(lax.all_to_all(parts, axis, 0, 0, tiled=True), axis=0)
    else:
        whole = lax.psum(rows, "trade")
        owned = lax.dynamic_slice_in_dim(
            whole, lax.axis_index("trade") * SETS_DEV, SETS_DEV, 0
        )

    decay = jnp.exp(-0.25 * reversion)[:, None]
    drift = ((1.0 - jnp.exp(-0.25 * reversion)) * long_level)[:, None]
    tenor = 0.25 * (jnp.arange(factors, dtype=jnp.float32) + 1.0)
    y_start = jnp.broadcast_to(initial_term_structure[:, None], (factors, paths))
    offsets = []
    powers = []
    running = jnp.zeros((factors, paths), jnp.float32)
    steady = jnp.zeros((factors, 1), jnp.float32)
    power = jnp.ones((factors, 1), jnp.float32)
    for step in range(section):
        moved = jnp.dot(mixing, shocks[step], precision=lax.Precision.HIGHEST)
        running = decay * running + drift + volatility[:, None] * moved
        steady = decay * steady + drift
        power = power * decay
        offsets.append(running)
        powers.append(power)
    multiplier = powers[-1]
    noise = (offsets[-1] - steady).astype(jnp.bfloat16)
    if Y_MODE == "permute":
        arrived = [None] + [
            from_behind(noise, "date", by).astype(jnp.float32)
            for by in range(1, dates_n)
        ]
    elif Y_MODE == "a2a":
        sent = jnp.broadcast_to(noise[None], (dates_n,) + noise.shape)
        got = lax.all_to_all(sent, "date", 0, 0, tiled=True)
        arrived = [None] + [
            lax.dynamic_index_in_dim(
                got, jnp.maximum(date_index - by, 0), 0, keepdims=False
            ).astype(jnp.float32)
            for by in range(1, dates_n)
        ]
    elif Y_MODE == "scan":
        arrived = None
    else:
        gathered = lax.all_gather(noise, "date", axis=0, tiled=False)
        arrived = [None] + [
            lax.dynamic_index_in_dim(
                gathered, jnp.maximum(date_index - by, 0), 0, keepdims=False
            ).astype(jnp.float32)
            for by in range(1, dates_n)
        ]
    incoming_state = y_start
    if Y_MODE == "scan":
        inclusive = noise.astype(jnp.float32)
        exclusive = jnp.zeros_like(inclusive)
        by = 1
        while by < dates_n:
            far = from_behind(inclusive.astype(jnp.bfloat16), "date", by).astype(jnp.float32)
            exclusive = exclusive + multiplier ** (by - 1) * far
            inclusive = inclusive + multiplier ** by * far
            by *= 2
        for by in range(dates_n - 1, 0, -1):
            stepped = multiplier * incoming_state + steady
            incoming_state = jnp.where(by <= date_index, stepped, incoming_state)
        incoming_state = incoming_state + exclusive
        if ORDER_TIE == "scan_first" and RS_MODE == "a2a":
            parts, incoming_state = lax.optimization_barrier((owned, incoming_state))
            owned = jnp.sum(lax.all_to_all(parts, TRADE_AXES[0], 0, 0, tiled=True), axis=0)
    for by in range(dates_n - 1, 0, -1) if Y_MODE != "scan" else ():
        stepped = multiplier * incoming_state + (steady + arrived[by])
        incoming_state = jnp.where(by <= date_index, stepped, incoming_state)

    values = []
    for step in range(section):
        y_now = powers[step] * incoming_state + offsets[step]
        discount = jnp.exp(-y_now * tenor[:, None]).astype(jnp.bfloat16).astype(jnp.float32)
        set_rows = owned[:, step * factors:(step + 1) * factors]
        value = jnp.dot(set_rows, discount, precision=lax.Precision.HIGHEST)
        values.append(jnp.mean(jnp.maximum(value, 0.0), axis=1))
    return jnp.stack(values)


def solution(mesh):
    trade = "trade"
    if TRADE_SPLIT:
        split = (mesh.devices.shape[1] // 2, 2) if TRADE_SPLIT == "pair" else TRADE_SPLIT
        devices = mesh.devices.reshape((mesh.devices.shape[0],) + split)
        mesh = jax.sharding.Mesh(devices, ("date",) + TRADE_AXES)
        trade = TRADE_AXES
    return jax.shard_map(
        per_device,
        mesh=mesh,
        in_specs=(
            P(),
            P(),
            P(),
            P(),
            P(),
            P("date", None, None),
            P(None, trade),
            P(trade),
            P(trade),
        ),
        out_specs=P("date", trade),
        check_vma=False,
    )
```
